128 devices in a mesh: dp: 8 (over x_lo, z), mp: 16 (over y, x_hi, core).
Axes of the slice: x: 4 (x_hi: 2, x_lo: 2; x = x_hi * 2 + x_lo), y: 4, z: 4, core: 2. Of those that a mesh axis runs over, the one named last changes fastest.
Arguments:
- tokens_in: bfloat16 [8192, 3072], P(('dp', 'mp')), may hold values from -6 to 6
- out_grad: bfloat16 [8192, 3072], P(('dp', 'mp')), may hold values from -0.29882812 to 0.29882812
- w_up: bfloat16 [12288, 3072], P('mp'), may hold values from -0.109375 to 0.109375
- w_down: bfloat16 [12288, 3072], P('mp'), may hold values from -0.0546875 to 0.0546875
- mask_up: int32 [96, 24], P('mp'), may hold values 0 or 1
- mask_down: int32 [96, 24], P('mp'), may hold values 0 or 1
- order_up: int32 [24], replicated, may hold values from 0 to 23, each once
- order_down: int32 [24], replicated, may hold values from 0 to 23, each once
- moment_one: float32 [2, 16, 24, 32, 3072], P(None, 'mp', 'dp'), may hold values from -1.8 to 1.8
- moment_two: float32 [2, 16, 24, 32, 3072], P(None, 'mp', 'dp'), may hold values from 0.03 to 1
Outputs:
- input_grad: bfloat16 [8192, 3072], P(('dp', 'mp'))
- update_step: bfloat16 [2, 12288, 3072], P(None, 'mp')
The draws below stay inside these ranges and needn't reach their ends.
Inputs may be any that keep to these rules, and one draw needn't show every extreme that they name: `order_up`: each value of 0 to 23 appears once. `order_down`: each value of 0 to 23 appears once.
All inputs are finite; a program needn't handle non-finite values. No bound on the sum of `mask_up` or of `mask_down` on one device may be relied on, other than what follows from the above.
Results may differ from the reference program's by a relative error of at most 0.014.
Values may be sent and summed in bfloat16 or wider, within the bound.
No kernel may reach another device: no remote copies, remote signals or barrier semaphores. Data moves between devices by JAX's collectives and lax.ppermute only.
A program may use at most 128 MiB of HBM per device.

```python
import math
import jax
import jax.numpy as jnp
from jax import lax

D = 3072
FFW = 12288
TOK_DEV = 64
BUCKET = 32
TOKENS = 8192
NBM = 24
OWNED = 3
N_DP = 8
N_MP = 16


def with_ends(array, key, low, largest):
    extent = array.shape
    spot = [jax.random.randint(jax.random.fold_in(key, axis), (), 0, extent[axis]) for axis in range(len(extent))]
    array = array.at[tuple(spot)].set(low)
    longest = extent.index(max(extent))
    spot[longest] = (spot[longest] + 1) % extent[longest]
    return array.at[tuple(spot)].set(largest)


def shard_levels(stream_key, extent, cuts, low, high):
    factor_of = 1.0
    for position, shards_of in cuts:
        draws = jax.random.uniform(jax.random.fold_in(jax.random.fold_in(stream_key, 6), position), (shards_of,), jnp.float32, low / len(cuts), high / len(cuts))
        factor_of = factor_of * jnp.repeat(jnp.exp(draws), extent[position] // shards_of).reshape((-1,) + (1,) * (len(extent) - 1 - position))
    return factor_of


def centred(stream_key, shape, spread, limit, shards=(), kind=jnp.bfloat16):
    array = jax.random.normal(stream_key, shape, jnp.float32) * spread
    if len(shards) > 0:
        array = shard_levels(stream_key, shape, shards, -0.22, 0.18) * array
    return jnp.clip(array, min=-limit, max=limit).astype(kind)


def setup_inputs(seed: int = 0) -> dict:
    key_of = jax.random.split(jax.random.key(seed), 11)
    return {
        "tokens_in": centred(key_of[0], (TOKENS, D), 1.0, 6.0, ((0, 128),)),
        "out_grad": centred(key_of[1], (TOKENS, D), 0.05, 0.29882812, ((0, 128),)),
        "w_up": centred(key_of[2], (FFW, D), D ** -0.5, 0.109375, ((0, 16),)),
        "w_down": centred(key_of[3], (FFW, D), FFW ** -0.5, 0.0546875, ((0, 16),)),
        "mask_up": with_ends((jax.random.randint(key_of[4], (FFW // 128, D // 128), 0, 2) < 1).astype(jnp.int32), jax.random.fold_in(key_of[4], 1), 0, 1),
        "mask_down": with_ends((jax.random.randint(key_of[5], (FFW // 128, D // 128), 0, 2) < 1).astype(jnp.int32), jax.random.fold_in(key_of[5], 1), 0, 1),
        "order_up": jax.random.permutation(key_of[6], NBM).astype(jnp.int32),
        "order_down": jax.random.permutation(key_of[7], NBM).astype(jnp.int32),
        "moment_one": centred(key_of[8], (2, N_MP, NBM, BUCKET, D), 0.3, 1.8, ((1, 16), (2, 8)), jnp.float32),
        "moment_two": jnp.clip(jnp.exp(math.log(1.0) - 3.506558 * jax.random.uniform(key_of[9], (2, N_MP, NBM, BUCKET, D), jnp.float32) ** shard_levels(key_of[9], (2, N_MP, NBM, BUCKET, D), ((1, 16), (2, 8)), -0.2, 0.2)), 0.03, 1.0),
    }


bias_first = 1.0 - 0.9 ** 10
bias_second = 1.0 - 0.95 ** 10

def expand_mask(blocks):
    block_rows, block_cols = blocks.shape
    wide = jnp.broadcast_to(blocks.astype(jnp.bfloat16)[:, None, :, None], (block_rows, 128, block_cols, 128))
    return wide.reshape(block_rows * 128, block_cols * 128)

def adam_step(summed, moment_a, moment_b, weight_rows, mask_rows):
    first_new = 0.9 * moment_a + 0.1 * summed
    second_new = 0.95 * moment_b + 0.05 * summed * summed
    update = first_new / bias_first / (jnp.sqrt(second_new / bias_second) + 1e-08)
    return (mask_rows * (update + 0.1 * weight_rows)).astype(jnp.bfloat16)

def owner_step(total, weight, keep, order_table, moment_one, moment_two, matrix):
    place = order_table % N_DP * OWNED + order_table // N_DP
    first_old = jnp.take(moment_one[matrix], place, axis=1)
    second_old = jnp.take(moment_two[matrix], place, axis=1)
    summed = total.reshape(N_MP, NBM, BUCKET, D)
    weight_rows = weight.astype(jnp.float32).reshape(N_MP, NBM, BUCKET, D)
    mask_rows = keep.astype(jnp.float32).reshape(N_MP, NBM, BUCKET, D)
    return adam_step(summed, first_old, second_old, weight_rows, mask_rows).reshape(FFW, D)

def reference(tokens_in, out_grad, w_up, w_down, mask_up, mask_down, order_up, order_down, moment_one, moment_two):
    keep_up = expand_mask(mask_up)
    keep_down = expand_mask(mask_down)
    up_live = w_up * keep_up
    down_live = w_down * keep_down
    group_rows = TOK_DEV * N_MP
    shard_width = FFW // N_MP
    grad_up = jnp.zeros((FFW, D), jnp.float32)
    grad_down = jnp.zeros((FFW, D), jnp.float32)
    input_parts = []
    for replica in range(N_DP):
        feat_rows = tokens_in[replica * group_rows:(replica + 1) * group_rows]
        grad_rows = out_grad[replica * group_rows:(replica + 1) * group_rows]
        hidden_pre = jnp.dot(feat_rows, up_live.T, preferred_element_type=jnp.float32)
        activation, gelu_back = jax.vjp(jax.nn.gelu, hidden_pre)
        act_low = activation.astype(jnp.bfloat16)
        part_down = (jnp.dot(act_low.T, grad_rows, preferred_element_type=jnp.float32) * keep_down).astype(jnp.bfloat16)
        act_grad = jnp.dot(grad_rows, down_live.T, preferred_element_type=jnp.float32)
        hidden_grad = gelu_back(act_grad)[0].astype(jnp.bfloat16)
        part_up = (jnp.dot(hidden_grad.T, feat_rows, preferred_element_type=jnp.float32) * keep_up).astype(jnp.bfloat16)
        grad_up = grad_up + lax.optimization_barrier(part_up).astype(jnp.float32)
        grad_down = grad_down + lax.optimization_barrier(part_down).astype(jnp.float32)
        input_total = jnp.zeros((group_rows, D), jnp.float32)
        for shard in range(N_MP):
            lo_unit = shard * shard_width
            partial_term = jnp.dot(hidden_grad[:, lo_unit:lo_unit + shard_width], up_live[lo_unit:lo_unit + shard_width], preferred_element_type=jnp.float32)
            input_total = input_total + lax.optimization_barrier(partial_term.astype(jnp.bfloat16)).astype(jnp.float32)
        input_parts.append(input_total.astype(jnp.bfloat16))
    step_up = owner_step(grad_up, w_up, keep_up, order_up, moment_one, moment_two, 0)
    step_down = owner_step(grad_down, w_down, keep_down, order_down, moment_one, moment_two, 1)
    return (jnp.concatenate(input_parts, axis=0), jnp.stack([step_up, step_down]))
```

```python
import jax
import jax.numpy as jnp
from jax import lax
from jax.sharding import PartitionSpec as P

bias_first = 1.0 - 0.9**10
bias_second = 1.0 - 0.95**10


def expand_mask(blocks):
    block_rows, block_cols = blocks.shape
    wide = jnp.broadcast_to(
        blocks.astype(jnp.bfloat16)[:, None, :, None], (block_rows, 128, block_cols, 128)
    )
    return wide.reshape(block_rows * 128, block_cols * 128)


def adam_step(summed, moment_a, moment_b, weight_rows, mask_rows):
    first_new = 0.9 * moment_a + 0.1 * summed
    second_new = 0.95 * moment_b + 0.05 * summed * summed
    update = first_new / bias_first / (jnp.sqrt(second_new / bias_second) + 1e-08)
    return (mask_rows * (update + 0.1 * weight_rows)).astype(jnp.bfloat16)


def slot_places(order_table, owners, owned):
    return order_table % owners * owned + order_table // owners


def shards(
    tokens_in,
    out_grad,
    w_up,
    w_down,
    mask_up,
    mask_down,
    order_up,
    order_down,
    moment_one,
    moment_two,
):
    owners = lax.axis_size("dp")
    hidden_local, width = w_up.shape
    buckets = order_up.shape[0]
    owned = buckets // owners
    bucket_rows = hidden_local // buckets
    keep_up = expand_mask(mask_up)
    keep_down = expand_mask(mask_down)
    up_live = w_up * keep_up
    down_live = w_down * keep_down
    place_up = slot_places(order_up, owners, owned)
    place_down = slot_places(order_down, owners, owned)
    sorter_up = jnp.argsort(place_up)
    sorter_down = jnp.argsort(place_down)

    def owner_order(matrix, sorter):
        return matrix.reshape(buckets, bucket_rows, width)[sorter]

    both_rows = lax.all_gather(jnp.stack([tokens_in, out_grad]), "mp", axis=1, tiled=True)
    feat_rows, grad_rows = both_rows[0], both_rows[1]
    hidden_pre = jnp.einsum("td,fd->tf", feat_rows, up_live, preferred_element_type=jnp.float32)
    activation, gelu_back = jax.vjp(jax.nn.gelu, hidden_pre)
    act_low = activation.astype(jnp.bfloat16)
    grad_down = (
        jnp.einsum("tf,td->fd", act_low, grad_rows, preferred_element_type=jnp.float32) * keep_down
    ).astype(jnp.bfloat16)
    down_sorted = owner_order(grad_down, sorter_down)
    act_grad = jnp.einsum("td,fd->tf", grad_rows, down_live, preferred_element_type=jnp.float32)
    hidden_grad = gelu_back(act_grad)[0].astype(jnp.bfloat16)
    grad_up = (
        jnp.einsum("tf,td->fd", hidden_grad, feat_rows, preferred_element_type=jnp.float32)
        * keep_up
    ).astype(jnp.bfloat16)
    up_sorted = owner_order(grad_up, sorter_up)
    by_owner = jnp.stack(
        [up_sorted.reshape(owners, owned, bucket_rows, width), down_sorted.reshape(owners, owned, bucket_rows, width)],
        axis=1,
    )
    summed = lax.psum_scatter(by_owner, "dp", scatter_dimension=0, tiled=True).astype(jnp.float32)
    up_summed, down_summed = summed[0, 0], summed[0, 1]
    partial_term = jnp.dot(hidden_grad, up_live, preferred_element_type=jnp.float32)
    input_grad = lax.psum_scatter(
        lax.optimization_barrier(partial_term.astype(jnp.bfloat16))
        .astype(jnp.float32)
        .astype(jnp.bfloat16),
        "mp",
        scatter_dimension=0,
        tiled=True,
    )
    owner_index = lax.axis_index("dp")

    def owned_rows(matrix, sorter):
        chosen = lax.dynamic_slice_in_dim(sorter, owner_index * owned, owned, 0)
        return matrix.reshape(buckets, bucket_rows, width)[chosen].astype(jnp.float32)

    step_up = adam_step(
        up_summed,
        moment_one[0, 0],
        moment_two[0, 0],
        owned_rows(w_up, sorter_up),
        owned_rows(keep_up, sorter_up),
    )
    step_down = adam_step(
        down_summed,
        moment_one[1, 0],
        moment_two[1, 0],
        owned_rows(w_down, sorter_down),
        owned_rows(keep_down, sorter_down),
    )
    stacked = jnp.stack([step_up, step_down])
    all_steps = lax.all_gather(stacked, "dp", axis=1, tiled=True)
    update_up = all_steps[0][place_up].reshape(hidden_local, width)
    update_down = all_steps[1][place_down].reshape(hidden_local, width)
    return (input_grad, jnp.stack([update_up, update_down]))


def solution(mesh):
    placed = (
        P(("dp", "mp"), None),
        P(("dp", "mp"), None),
        P("mp", None),
        P("mp", None),
        P("mp", None),
        P("mp", None),
        P(),
        P(),
        P(None, "mp", "dp", None, None),
        P(None, "mp", "dp", None, None),
    )
    return jax.shard_map(
        shards,
        mesh=mesh,
        in_specs=placed,
        out_specs=(P(("dp", "mp"), None), P(None, "mp", None)),
        check_vma=False,
    )
```

```python
import jax
import jax.numpy as jnp
from jax import lax
from jax.sharding import PartitionSpec as P


bias_first = 1.0 - 0.9**10
bias_second = 1.0 - 0.95**10


def expand_mask(blocks):
    block_rows, block_cols = blocks.shape
    wide = jnp.broadcast_to(
        blocks.astype(jnp.bfloat16)[:, None, :, None], (block_rows, 128, block_cols, 128)
    )
    return wide.reshape(block_rows * 128, block_cols * 128)


def adam_step(summed, moment_a, moment_b, weight_rows, mask_rows):
    first_new = 0.9 * moment_a + 0.1 * summed
    second_new = 0.95 * moment_b + 0.05 * summed * summed
    update = first_new / bias_first / (jnp.sqrt(second_new / bias_second) + 1e-08)
    return (mask_rows * (update + 0.1 * weight_rows)).astype(jnp.bfloat16)


def slot_places(order_table, owners, owned):
    return order_table % owners * owned + order_table // owners


def layer(
    tokens_in,
    out_grad,
    w_up,
    w_down,
    mask_up,
    mask_down,
    order_up,
    order_down,
    moment_one,
    moment_two,
):
    owners = lax.axis_size("dp")
    hidden_local, width = w_up.shape
    buckets = order_up.shape[0]
    owned = buckets // owners
    bucket_rows = hidden_local // buckets
    local_rows = tokens_in.shape[0]
    half = local_rows // 2
    place_up = slot_places(order_up, owners, owned)
    place_down = slot_places(order_down, owners, owned)
    sorter_up = jnp.argsort(place_up)
    sorter_down = jnp.argsort(place_down)

    def owner_order(matrix, sorter):
        return matrix.reshape(buckets, bucket_rows, width)[sorter].reshape(hidden_local, width)

    keep_up = owner_order(expand_mask(mask_up), sorter_up)
    keep_down = owner_order(expand_mask(mask_down), sorter_up)
    w_up_s = owner_order(w_up, sorter_up)
    w_down_s = owner_order(w_down, sorter_up)
    up_live = w_up_s * keep_up
    down_live = w_down_s * keep_down
    down_from_up = jnp.argsort(sorter_up)[sorter_down]

    def gather_rows(lo):
        both = jnp.stack([tokens_in[lo : lo + half], out_grad[lo : lo + half]])
        rows = lax.all_gather(both, "mp", axis=1, tiled=True)
        return rows[0], rows[1]

    def piece(feat_rows, grad_rows):
      hidden_pre = jnp.einsum("td,fd->tf", feat_rows, up_live, preferred_element_type=jnp.float32)
      activation, gelu_back = jax.vjp(jax.nn.gelu, hidden_pre)
      act_low = activation.astype(jnp.bfloat16)
      down_part = jnp.einsum("tf,td->fd", act_low, grad_rows, preferred_element_type=jnp.float32)
      act_grad = jnp.einsum("td,fd->tf", grad_rows, down_live, preferred_element_type=jnp.float32)
      hidden_grad = gelu_back(act_grad)[0].astype(jnp.bfloat16)
      up_part = jnp.einsum("tf,td->fd", hidden_grad, feat_rows, preferred_element_type=jnp.float32)
      partial_term = jnp.dot(hidden_grad, up_live, preferred_element_type=jnp.float32)
      input_part = lax.psum_scatter(
          lax.optimization_barrier(partial_term.astype(jnp.bfloat16))
          .astype(jnp.float32)
          .astype(jnp.bfloat16),
          "mp",
          scatter_dimension=0,
          tiled=True,
      )
      return up_part, down_part, input_part

    feat_a, grad_a = gather_rows(0)
    feat_b, grad_b = gather_rows(half)
    up_a, down_a, input_a = piece(feat_a, grad_a)
    up_b, down_b, input_b = piece(feat_b, grad_b)
    grad_up = ((up_a + up_b) * keep_up).astype(jnp.bfloat16)
    grad_down = ((down_a + down_b) * keep_down).astype(jnp.bfloat16)

    by_owner = jnp.stack(
        [
            grad_up.reshape(owners, owned, bucket_rows, width),
            grad_down.reshape(buckets, bucket_rows, width)[down_from_up].reshape(owners, owned, bucket_rows, width),
        ],
        axis=1,
    )
    summed = lax.psum_scatter(by_owner, "dp", scatter_dimension=0, tiled=True).astype(jnp.float32)
    up_summed, down_summed = summed[0, 0], summed[0, 1]
    owner_index = lax.axis_index("dp")

    def owned_rows(matrix, sorter):
        chosen = lax.dynamic_slice_in_dim(sorter, owner_index * owned, owned, 0)
        return matrix.reshape(buckets, bucket_rows, width)[chosen].astype(jnp.float32)

    step_up = adam_step(
        up_summed,
        moment_one[0, 0],
        moment_two[0, 0],
        owned_rows(w_up, sorter_up),
        owned_rows(expand_mask(mask_up), sorter_up),
    )
    step_down = adam_step(
        down_summed,
        moment_one[1, 0],
        moment_two[1, 0],
        owned_rows(w_down, sorter_down),
        owned_rows(expand_mask(mask_down), sorter_down),
    )
    stacked = jnp.stack([step_up, step_down])
    all_steps = lax.all_gather(stacked, "dp", axis=1, tiled=True)
    update_up = all_steps[0][place_up].reshape(hidden_local, width)
    update_down = all_steps[1][place_down].reshape(hidden_local, width)
    input_grad = jnp.concatenate([input_a, input_b], axis=0)
    return (input_grad, jnp.stack([update_up, update_down]))


def solution(mesh):
    placed = (
        P(("dp", "mp"), None),
        P(("dp", "mp"), None),
        P("mp", None),
        P("mp", None),
        P("mp", None),
        P("mp", None),
        P(),
        P(),
        P(None, "mp", "dp", None, None),
        P(None, "mp", "dp", None, None),
    )
    return jax.shard_map(
        layer,
        mesh=mesh,
        in_specs=placed,
        out_specs=(P(("dp", "mp"), None), P(None, "mp", None)),
        check_vma=False,
    )
```

```python
import jax
import jax.numpy as jnp
from jax import lax
from jax.sharding import PartitionSpec as P


bias_first = 1.0 - 0.9**10
bias_second = 1.0 - 0.95**10


def expand_mask(blocks):
    block_rows, block_cols = blocks.shape
    wide = jnp.broadcast_to(
        blocks.astype(jnp.bfloat16)[:, None, :, None], (block_rows, 128, block_cols, 128)
    )
    return wide.reshape(block_rows * 128, block_cols * 128)


def adam_step(summed, moment_a, moment_b, weight_rows, mask_rows):
    first_new = 0.9 * moment_a + 0.1 * summed
    second_new = 0.95 * moment_b + 0.05 * summed * summed
    update = first_new / bias_first / (jnp.sqrt(second_new / bias_second) + 1e-08)
    return (mask_rows * (update + 0.1 * weight_rows)).astype(jnp.bfloat16)


def slot_places(order_table, owners, owned):
    return order_table % owners * owned + order_table // owners


def layer(
    tokens_in,
    out_grad,
    w_up,
    w_down,
    mask_up,
    mask_down,
    order_up,
    order_down,
    moment_one,
    moment_two,
):
    owners = lax.axis_size("dp")
    hidden_local, width = w_up.shape
    buckets = order_up.shape[0]
    owned = buckets // owners
    bucket_rows = hidden_local // buckets
    keep_up = expand_mask(mask_up)
    keep_down = expand_mask(mask_down)
    up_live = w_up * keep_up
    down_live = w_down * keep_down
    place_up = slot_places(order_up, owners, owned)
    place_down = slot_places(order_down, owners, owned)
    sorter_up = jnp.argsort(place_up)
    sorter_down = jnp.argsort(place_down)

    def owner_order(matrix, sorter):
        return matrix.reshape(buckets, bucket_rows, width)[sorter]

    both_rows = lax.all_gather(jnp.stack([tokens_in, out_grad]), "mp", axis=1, tiled=True)
    feat_rows, grad_rows = both_rows[0], both_rows[1]
    hidden_pre = jnp.einsum("td,fd->tf", feat_rows, up_live, preferred_element_type=jnp.float32)
    activation, gelu_back = jax.vjp(jax.nn.gelu, hidden_pre)
    act_low = activation.astype(jnp.bfloat16)
    grad_down = (
        jnp.einsum("tf,td->fd", act_low, grad_rows, preferred_element_type=jnp.float32) * keep_down
    ).astype(jnp.bfloat16)
    down_sorted = owner_order(grad_down, sorter_down)
    act_grad = jnp.einsum("td,fd->tf", grad_rows, down_live, preferred_element_type=jnp.float32)
    hidden_grad = gelu_back(act_grad)[0].astype(jnp.bfloat16)
    grad_up = (
        jnp.einsum("tf,td->fd", hidden_grad, feat_rows, preferred_element_type=jnp.float32)
        * keep_up
    ).astype(jnp.bfloat16)
    up_sorted = owner_order(grad_up, sorter_up)
    down_summed = lax.psum_scatter(down_sorted, "dp", scatter_dimension=0, tiled=True).astype(jnp.float32)
    up_summed = lax.psum_scatter(up_sorted, "dp", scatter_dimension=0, tiled=True).astype(jnp.float32)
    partial_term = jnp.dot(hidden_grad, up_live, preferred_element_type=jnp.float32)
    input_grad = lax.psum_scatter(
        lax.optimization_barrier(partial_term.astype(jnp.bfloat16))
        .astype(jnp.float32)
        .astype(jnp.bfloat16),
        "mp",
        scatter_dimension=0,
        tiled=True,
    )
    owner_index = lax.axis_index("dp")

    def owned_rows(matrix, sorter):
        chosen = lax.dynamic_slice_in_dim(sorter, owner_index * owned, owned, 0)
        return matrix.reshape(buckets, bucket_rows, width)[chosen].astype(jnp.float32)

    step_up = adam_step(
        up_summed,
        moment_one[0, 0],
        moment_two[0, 0],
        owned_rows(w_up, sorter_up),
        owned_rows(keep_up, sorter_up),
    )
    step_down = adam_step(
        down_summed,
        moment_one[1, 0],
        moment_two[1, 0],
        owned_rows(w_down, sorter_down),
        owned_rows(keep_down, sorter_down),
    )
    stacked = jnp.stack([step_up, step_down])
    all_steps = lax.all_gather(stacked, "dp", axis=1, tiled=True)
    update_up = all_steps[0][place_up].reshape(hidden_local, width)
    update_down = all_steps[1][place_down].reshape(hidden_local, width)
    return (input_grad, jnp.stack([update_up, update_down]))


def solution(mesh):
    placed = (
        P(("dp", "mp"), None),
        P(("dp", "mp"), None),
        P("mp", None),
        P("mp", None),
        P("mp", None),
        P("mp", None),
        P(),
        P(),
        P(None, "mp", "dp", None, None),
        P(None, "mp", "dp", None, None),
    )
    return jax.shard_map(
        layer,
        mesh=mesh,
        in_specs=placed,
        out_specs=(P(("dp", "mp"), None), P(None, "mp", None)),
        check_vma=False,
    )
```

```python
import jax
import jax.numpy as jnp
from jax import lax
from jax.sharding import PartitionSpec as P


bias_first = 1.0 - 0.9**10
bias_second = 1.0 - 0.95**10


def expand_mask(blocks):
    block_rows, block_cols = blocks.shape
    wide = jnp.broadcast_to(
        blocks.astype(jnp.bfloat16)[:, None, :, None], (block_rows, 128, block_cols, 128)
    )
    return wide.reshape(block_rows * 128, block_cols * 128)


def adam_step(summed, moment_a, moment_b, weight_rows, mask_rows):
    first_new = 0.9 * moment_a + 0.1 * summed
    second_new = 0.95 * moment_b + 0.05 * summed * summed
    update = first_new / bias_first / (jnp.sqrt(second_new / bias_second) + 1e-08)
    return (mask_rows * (update + 0.1 * weight_rows)).astype(jnp.bfloat16)


def slot_places(order_table, owners, owned):
    return order_table % owners * owned + order_table // owners


def layer(
    tokens_in,
    out_grad,
    w_up,
    w_down,
    mask_up,
    mask_down,
    order_up,
    order_down,
    moment_one,
    moment_two,
):
    owners = lax.axis_size("dp")
    hidden_local, width = w_up.shape
    buckets = order_up.shape[0]
    owned = buckets // owners
    bucket_rows = hidden_local // buckets
    keep_up = expand_mask(mask_up)
    keep_down = expand_mask(mask_down)
    place_up = slot_places(order_up, owners, owned)
    place_down = slot_places(order_down, owners, owned)
    sorter_up = jnp.argsort(place_up)
    sorter_down = jnp.argsort(place_down)

    def owner_order(matrix, sorter):
        return matrix.reshape(buckets, bucket_rows, width)[sorter]

    def down_layout(matrix):
        return owner_order(matrix, sorter_down).reshape(hidden_local, width)

    keep_up_s = down_layout(keep_up)
    keep_down_s = down_layout(keep_down)
    up_live = down_layout(w_up) * keep_up_s
    down_live = down_layout(w_down) * keep_down_s
    up_from_down = jnp.argsort(sorter_down)[sorter_up]

    both_rows = lax.all_gather(jnp.stack([tokens_in, out_grad]), "mp", axis=1, tiled=True)
    feat_rows, grad_rows = both_rows[0], both_rows[1]
    hidden_pre = jnp.einsum("td,fd->tf", feat_rows, up_live, preferred_element_type=jnp.float32)
    activation, gelu_back = jax.vjp(jax.nn.gelu, hidden_pre)
    act_low = activation.astype(jnp.bfloat16)
    grad_down = (
        jnp.einsum("tf,td->fd", act_low, grad_rows, preferred_element_type=jnp.float32) * keep_down_s
    ).astype(jnp.bfloat16)
    down_sorted = grad_down.reshape(buckets, bucket_rows, width)
    act_grad = jnp.einsum("td,fd->tf", grad_rows, down_live, preferred_element_type=jnp.float32)
    hidden_grad = gelu_back(act_grad)[0].astype(jnp.bfloat16)
    grad_up = (
        jnp.einsum("tf,td->fd", hidden_grad, feat_rows, preferred_element_type=jnp.float32)
        * keep_up_s
    ).astype(jnp.bfloat16)
    up_sorted = owner_order(grad_up, up_from_down)
    down_summed = lax.psum_scatter(down_sorted, "dp", scatter_dimension=0, tiled=True).astype(jnp.float32)
    up_summed = lax.psum_scatter(up_sorted, "dp", scatter_dimension=0, tiled=True).astype(jnp.float32)
    partial_term = jnp.dot(hidden_grad, up_live, preferred_element_type=jnp.float32)
    input_grad = lax.psum_scatter(
        lax.optimization_barrier(partial_term.astype(jnp.bfloat16))
        .astype(jnp.float32)
        .astype(jnp.bfloat16),
        "mp",
        scatter_dimension=0,
        tiled=True,
    )
    owner_index = lax.axis_index("dp")

    def owned_rows(matrix, sorter):
        chosen = lax.dynamic_slice_in_dim(sorter, owner_index * owned, owned, 0)
        return matrix.reshape(buckets, bucket_rows, width)[chosen].astype(jnp.float32)

    step_up = adam_step(
        up_summed,
        moment_one[0, 0],
        moment_two[0, 0],
        owned_rows(w_up, sorter_up),
        owned_rows(keep_up, sorter_up),
    )
    step_down = adam_step(
        down_summed,
        moment_one[1, 0],
        moment_two[1, 0],
        owned_rows(w_down, sorter_down),
        owned_rows(keep_down, sorter_down),
    )
    stacked = jnp.stack([step_up, step_down])
    all_steps = lax.all_gather(stacked, "dp", axis=1, tiled=True)
    update_up = all_steps[0][place_up].reshape(hidden_local, width)
    update_down = all_steps[1][place_down].reshape(hidden_local, width)
    return (input_grad, jnp.stack([update_up, update_down]))


def solution(mesh):
    placed = (
        P(("dp", "mp"), None),
        P(("dp", "mp"), None),
        P("mp", None),
        P("mp", None),
        P("mp", None),
        P("mp", None),
        P(),
        P(),
        P(None, "mp", "dp", None, None),
        P(None, "mp", "dp", None, None),
    )
    return jax.shard_map(
        layer,
        mesh=mesh,
        in_specs=placed,
        out_specs=(P(("dp", "mp"), None), P(None, "mp", None)),
        check_vma=False,
    )
```

```python
import jax
import jax.numpy as jnp
from jax import lax
from jax.sharding import PartitionSpec as P


bias_first = 1.0 - 0.9**10
bias_second = 1.0 - 0.95**10


def expand_mask(blocks):
    block_rows, block_cols = blocks.shape
    wide = jnp.broadcast_to(
        blocks.astype(jnp.bfloat16)[:, None, :, None], (block_rows, 128, block_cols, 128)
    )
    return wide.reshape(block_rows * 128, block_cols * 128)


def adam_step(summed, moment_a, moment_b, weight_rows, mask_rows):
    first_new = 0.9 * moment_a + 0.1 * summed
    second_new = 0.95 * moment_b + 0.05 * summed * summed
    update = first_new / bias_first / (jnp.sqrt(second_new / bias_second) + 1e-08)
    return (mask_rows * (update + 0.1 * weight_rows)).astype(jnp.bfloat16)


def slot_places(order_table, owners, owned):
    return order_table % owners * owned + order_table // owners


def layer(
    tokens_in,
    out_grad,
    w_up,
    w_down,
    mask_up,
    mask_down,
    order_up,
    order_down,
    moment_one,
    moment_two,
):
    owners = lax.axis_size("dp")
    local_rows = tokens_in.shape[0]
    hidden_local, width = w_up.shape
    buckets = order_up.shape[0]
    owned = buckets // owners
    bucket_rows = hidden_local // buckets
    keep_up = expand_mask(mask_up)
    keep_down = expand_mask(mask_down)
    place_up = slot_places(order_up, owners, owned)
    place_down = slot_places(order_down, owners, owned)
    sorter_up = jnp.argsort(place_up)
    sorter_down = jnp.argsort(place_down)

    def owner_order(matrix, sorter):
        return matrix.reshape(buckets, bucket_rows, width)[sorter]

    def down_layout(matrix):
        return owner_order(matrix, sorter_down).reshape(hidden_local, width)

    keep_up_s = down_layout(keep_up)
    keep_down_s = down_layout(keep_down)
    up_live = down_layout(w_up) * keep_up_s
    down_live = down_layout(w_down) * keep_down_s
    up_from_down = jnp.argsort(sorter_down)[sorter_up]

    both_rows = lax.all_gather(jnp.stack([tokens_in, out_grad]), "mp", axis=1, tiled=True)
    feat_rows, grad_rows = both_rows[0], both_rows[1]
    hidden_pre = jnp.einsum("td,fd->tf", feat_rows, up_live, preferred_element_type=jnp.float32)
    activation, gelu_back = jax.vjp(jax.nn.gelu, hidden_pre)
    act_low = activation.astype(jnp.bfloat16)
    grad_down = (
        jnp.einsum("tf,td->fd", act_low, grad_rows, preferred_element_type=jnp.float32) * keep_down_s
    ).astype(jnp.bfloat16)
    down_sorted = grad_down.reshape(buckets, bucket_rows, width)
    act_grad = jnp.einsum("td,fd->tf", grad_rows, down_live, preferred_element_type=jnp.float32)
    hidden_grad = gelu_back(act_grad)[0].astype(jnp.bfloat16)
    grad_up = (
        jnp.einsum("tf,td->fd", hidden_grad, feat_rows, preferred_element_type=jnp.float32)
        * keep_up_s
    ).astype(jnp.bfloat16)
    up_sorted = owner_order(grad_up, up_from_down)
    down_summed = lax.psum_scatter(down_sorted, "dp", scatter_dimension=0, tiled=True).astype(jnp.float32)
    up_summed = lax.psum_scatter(up_sorted, "dp", scatter_dimension=0, tiled=True).astype(jnp.float32)
    partial_term = jnp.dot(hidden_grad, up_live, preferred_element_type=jnp.float32)
    shards_mp = lax.axis_size("mp")
    shares = lax.all_to_all(
        partial_term.astype(jnp.bfloat16).reshape(shards_mp, local_rows, width), "mp", 0, 0, tiled=True
    )
    input_grad = shares.astype(jnp.float32).sum(axis=0).astype(jnp.bfloat16)
    owner_index = lax.axis_index("dp")

    def owned_rows(matrix, sorter):
        chosen = lax.dynamic_slice_in_dim(sorter, owner_index * owned, owned, 0)
        return matrix.reshape(buckets, bucket_rows, width)[chosen].astype(jnp.float32)

    step_up = adam_step(
        up_summed,
        moment_one[0, 0],
        moment_two[0, 0],
        owned_rows(w_up, sorter_up),
        owned_rows(keep_up, sorter_up),
    )
    step_down = adam_step(
        down_summed,
        moment_one[1, 0],
        moment_two[1, 0],
        owned_rows(w_down, sorter_down),
        owned_rows(keep_down, sorter_down),
    )
    stacked = jnp.stack([step_up, step_down])
    all_steps = lax.all_gather(stacked, "dp", axis=1, tiled=True)
    update_up = all_steps[0][place_up].reshape(hidden_local, width)
    update_down = all_steps[1][place_down].reshape(hidden_local, width)
    return (input_grad, jnp.stack([update_up, update_down]))


def solution(mesh):
    placed = (
        P(("dp", "mp"), None),
        P(("dp", "mp"), None),
        P("mp", None),
        P("mp", None),
        P("mp", None),
        P("mp", None),
        P(),
        P(),
        P(None, "mp", "dp", None, None),
        P(None, "mp", "dp", None, None),
    )
    return jax.shard_map(
        layer,
        mesh=mesh,
        in_specs=placed,
        out_specs=(P(("dp", "mp"), None), P(None, "mp", None)),
        check_vma=False,
    )
```

```python
import jax
import jax.numpy as jnp
from jax import lax
from jax.sharding import PartitionSpec as P


bias_first = 1.0 - 0.9**10
bias_second = 1.0 - 0.95**10


def expand_mask(blocks):
    block_rows, block_cols = blocks.shape
    wide = jnp.broadcast_to(
        blocks.astype(jnp.bfloat16)[:, None, :, None], (block_rows, 128, block_cols, 128)
    )
    return wide.reshape(block_rows * 128, block_cols * 128)


def adam_step(summed, moment_a, moment_b, weight_rows, mask_rows):
    first_new = 0.9 * moment_a + 0.1 * summed
    second_new = 0.95 * moment_b + 0.05 * summed * summed
    update = first_new / bias_first / (jnp.sqrt(second_new / bias_second) + 1e-08)
    return (mask_rows * (update + 0.1 * weight_rows)).astype(jnp.bfloat16)


def slot_places(order_table, owners, owned):
    return order_table % owners * owned + order_table // owners


def layer(
    tokens_in,
    out_grad,
    w_up,
    w_down,
    mask_up,
    mask_down,
    order_up,
    order_down,
    moment_one,
    moment_two,
):
    owners = lax.axis_size("dp")
    local_rows = tokens_in.shape[0]
    hidden_local, width = w_up.shape
    buckets = order_up.shape[0]
    owned = buckets // owners
    bucket_rows = hidden_local // buckets
    keep_up = expand_mask(mask_up)
    keep_down = expand_mask(mask_down)
    place_up = slot_places(order_up, owners, owned)
    place_down = slot_places(order_down, owners, owned)
    sorter_up = jnp.argsort(place_up)
    sorter_down = jnp.argsort(place_down)

    def owner_order(matrix, sorter):
        return matrix.reshape(buckets, bucket_rows, width)[sorter]

    def down_layout(matrix):
        return owner_order(matrix, sorter_down).reshape(hidden_local, width)

    keep_up_s = down_layout(keep_up)
    keep_down_s = down_layout(keep_down)
    up_live = down_layout(w_up) * keep_up_s
    down_live = down_layout(w_down) * keep_down_s
    up_from_down = jnp.argsort(sorter_down)[sorter_up]

    both_rows = lax.all_gather(jnp.stack([tokens_in, out_grad]), "mp", axis=1, tiled=True)
    feat_rows, grad_rows = both_rows[0], both_rows[1]
    hidden_pre = jnp.einsum("td,fd->tf", feat_rows, up_live, preferred_element_type=jnp.float32)
    activation, gelu_back = jax.vjp(jax.nn.gelu, hidden_pre)
    act_low = activation.astype(jnp.bfloat16)
    grad_down = (
        jnp.einsum("tf,td->fd", act_low, grad_rows, preferred_element_type=jnp.float32) * keep_down_s
    ).astype(jnp.bfloat16)
    down_sorted = grad_down.reshape(buckets, bucket_rows, width)
    act_grad = jnp.einsum("td,fd->tf", grad_rows, down_live, preferred_element_type=jnp.float32)
    hidden_grad = gelu_back(act_grad)[0].astype(jnp.bfloat16)
    grad_up = (
        jnp.einsum("tf,td->fd", hidden_grad, feat_rows, preferred_element_type=jnp.float32)
        * keep_up_s
    ).astype(jnp.bfloat16)
    up_sorted = owner_order(grad_up, up_from_down)
    down_summed = lax.psum_scatter(down_sorted, "dp", scatter_dimension=0, tiled=True).astype(jnp.float32)
    up_summed = lax.psum_scatter(up_sorted, "dp", scatter_dimension=0, tiled=True).astype(jnp.float32)
    partial_term = jnp.dot(hidden_grad, up_live, preferred_element_type=jnp.float32)
    shards_mp = lax.axis_size("mp")
    shares = lax.all_to_all(
        partial_term.astype(jnp.bfloat16).reshape(shards_mp, local_rows, width), "mp", 0, 0, tiled=True
    )
    input_grad = shares.astype(jnp.float32).sum(axis=0).astype(jnp.bfloat16)
    owner_index = lax.axis_index("dp")

    def owned_rows(matrix, sorter):
        chosen = lax.dynamic_slice_in_dim(sorter, owner_index * owned, owned, 0)
        return matrix.reshape(buckets, bucket_rows, width)[chosen].astype(jnp.float32)

    step_up = adam_step(
        up_summed,
        moment_one[0, 0],
        moment_two[0, 0],
        owned_rows(w_up, sorter_up),
        owned_rows(keep_up, sorter_up),
    )
    step_down = adam_step(
        down_summed,
        moment_one[1, 0],
        moment_two[1, 0],
        owned_rows(w_down, sorter_down),
        owned_rows(keep_down, sorter_down),
    )
    stacked = jnp.stack([step_up, step_down])
    all_steps = lax.all_gather(stacked, "dp", axis=1, tiled=True)
    places = jnp.concatenate([place_up, place_down + buckets])
    updates = all_steps.reshape(2 * buckets, bucket_rows, width)[places]
    return (input_grad, updates.reshape(2, hidden_local, width))


def solution(mesh):
    placed = (
        P(("dp", "mp"), None),
        P(("dp", "mp"), None),
        P("mp", None),
        P("mp", None),
        P("mp", None),
        P("mp", None),
        P(),
        P(),
        P(None, "mp", "dp", None, None),
        P(None, "mp", "dp", None, None),
    )
    return jax.shard_map(
        layer,
        mesh=mesh,
        in_specs=placed,
        out_specs=(P(("dp", "mp"), None), P(None, "mp", None)),
        check_vma=False,
    )
```

```python
import jax
import jax.numpy as jnp
from jax import lax
from jax.sharding import PartitionSpec as P


bias_first = 1.0 - 0.9**10
bias_second = 1.0 - 0.95**10


def expand_mask(blocks):
    block_rows, block_cols = blocks.shape
    wide = jnp.broadcast_to(
        blocks.astype(jnp.bfloat16)[:, None, :, None], (block_rows, 128, block_cols, 128)
    )
    return wide.reshape(block_rows * 128, block_cols * 128)


def adam_step(summed, moment_a, moment_b, weight_rows, mask_rows):
    first_new = 0.9 * moment_a + 0.1 * summed
    second_new = 0.95 * moment_b + 0.05 * summed * summed
    update = first_new / bias_first / (jnp.sqrt(second_new / bias_second) + 1e-08)
    return (mask_rows * (update + 0.1 * weight_rows)).astype(jnp.bfloat16)


def slot_places(order_table, owners, owned):
    return order_table % owners * owned + order_table // owners


def layer(
    tokens_in,
    out_grad,
    w_up,
    w_down,
    mask_up,
    mask_down,
    order_up,
    order_down,
    moment_one,
    moment_two,
):
    owners = lax.axis_size("dp")
    local_rows = tokens_in.shape[0]
    hidden_local, width = w_up.shape
    buckets = order_up.shape[0]
    owned = buckets // owners
    bucket_rows = hidden_local // buckets
    keep_up = expand_mask(mask_up)
    keep_down = expand_mask(mask_down)
    place_up = slot_places(order_up, owners, owned)
    place_down = slot_places(order_down, owners, owned)
    sorter_up = jnp.argsort(place_up)
    sorter_down = jnp.argsort(place_down)

    def owner_order(matrix, sorter):
        return matrix.reshape(buckets, bucket_rows, width)[sorter]

    def down_layout(matrix):
        return owner_order(matrix, sorter_down).reshape(hidden_local, width)

    keep_up_s = down_layout(keep_up)
    keep_down_s = down_layout(keep_down)
    up_live = down_layout(w_up) * keep_up_s
    down_live = down_layout(w_down) * keep_down_s
    up_from_down = jnp.argsort(sorter_down)[sorter_up]

    both_rows = lax.all_gather(jnp.stack([tokens_in, out_grad]), "mp", axis=1, tiled=True)
    feat_rows, grad_rows = both_rows[0], both_rows[1]
    hidden_pre = jnp.einsum("td,fd->tf", feat_rows, up_live, preferred_element_type=jnp.float32)
    activation, gelu_back = jax.vjp(jax.nn.gelu, hidden_pre)
    act_low = activation.astype(jnp.bfloat16)
    grad_down = (
        jnp.einsum("tf,td->fd", act_low, grad_rows, preferred_element_type=jnp.float32) * keep_down_s
    ).astype(jnp.bfloat16)
    down_sorted = grad_down.reshape(buckets, bucket_rows, width)
    act_grad = jnp.einsum("td,fd->tf", grad_rows, down_live, preferred_element_type=jnp.float32)
    hidden_grad = gelu_back(act_grad)[0].astype(jnp.bfloat16)
    grad_up = (
        jnp.einsum("tf,td->fd", hidden_grad, feat_rows, preferred_element_type=jnp.float32)
        * keep_up_s
    ).astype(jnp.bfloat16)
    up_sorted = owner_order(grad_up, up_from_down)
    down_summed = lax.psum_scatter(down_sorted, "dp", scatter_dimension=0, tiled=True).astype(jnp.float32)
    up_summed = lax.psum_scatter(up_sorted, "dp", scatter_dimension=0, tiled=True).astype(jnp.float32)
    partial_term = jnp.dot(hidden_grad, up_live, preferred_element_type=jnp.float32)
    shards_mp = lax.axis_size("mp")
    shares = lax.all_to_all(
        partial_term.astype(jnp.bfloat16).reshape(shards_mp, local_rows, width), "mp", 0, 0, tiled=True
    )
    input_grad = shares.astype(jnp.float32).sum(axis=0).astype(jnp.bfloat16)
    owner_index = lax.axis_index("dp")

    def owned_rows(matrix, sorter):
        chosen = lax.dynamic_slice_in_dim(sorter, owner_index * owned, owned, 0)
        return matrix.reshape(buckets, bucket_rows, width)[chosen].astype(jnp.float32)

    step_up = adam_step(
        up_summed,
        moment_one[0, 0],
        moment_two[0, 0],
        owned_rows(w_up, sorter_up),
        owned_rows(keep_up, sorter_up),
    )
    step_down = adam_step(
        down_summed,
        moment_one[1, 0],
        moment_two[1, 0],
        owned_rows(w_down, sorter_down),
        owned_rows(keep_down, sorter_down),
    )
    stacked = jnp.stack([step_up, step_down])
    all_steps = lax.all_gather(stacked, "dp", axis=1, tiled=True)
    places = jnp.stack([place_up, place_down])
    chooser = (places[:, :, None] == jnp.arange(buckets)[None, None, :]).astype(jnp.bfloat16)
    updates = jnp.einsum(
        "sbk,skx->sbx",
        chooser,
        all_steps.reshape(2, buckets, bucket_rows * width),
        preferred_element_type=jnp.float32,
    ).astype(jnp.bfloat16)
    return (input_grad, updates.reshape(2, hidden_local, width))


def solution(mesh):
    placed = (
        P(("dp", "mp"), None),
        P(("dp", "mp"), None),
        P("mp", None),
        P("mp", None),
        P("mp", None),
        P("mp", None),
        P(),
        P(),
        P(None, "mp", "dp", None, None),
        P(None, "mp", "dp", None, None),
    )
    return jax.shard_map(
        layer,
        mesh=mesh,
        in_specs=placed,
        out_specs=(P(("dp", "mp"), None), P(None, "mp", None)),
        check_vma=False,
    )
```
